512 devices in a mesh: section: 32 (over y, z_lo, core), tensor: 16 (over x, z_hi).
Axes of the slice: x: 4, y: 8, z: 8 (z_hi: 4, z_lo: 2; z = z_hi * 2 + z_lo), core: 2. Of those that a mesh axis runs over, the one named last changes fastest.
Arguments:
- tokens: bfloat16 [768, 8192], P('section', 'tensor'), may hold values from -6 to 6
- out_grad: bfloat16 [768, 8192], P('section', 'tensor'), may hold values from -3 to 3
- gate_weight: bfloat16 [8192, 14336], P('tensor', 'section'), may hold values from -0.0625 to 0.0625
- up_weight: bfloat16 [8192, 14336], P('tensor', 'section'), may hold values from -0.0625 to 0.0625
- down_weight: bfloat16 [14336, 8192], P('section', 'tensor'), may hold values from -0.046875 to 0.046875
Outputs:
- grad_input: bfloat16 [768, 8192], P('section', 'tensor')
- grad_gate: bfloat16 [8192, 14336], P('tensor', 'section')
- grad_up: bfloat16 [8192, 14336], P('tensor', 'section')
- grad_down: bfloat16 [14336, 8192], P('section', 'tensor')
The draws below stay inside these ranges and needn't reach their ends.
All inputs are finite; a program needn't handle non-finite values.
Results may differ from the reference program's by a relative error of at most 0.0049.
Values may be sent and summed in bfloat16 or wider, within the bound.
No kernel may reach another device: no remote copies, remote signals or barrier semaphores. Data moves between devices by JAX's collectives and lax.ppermute only.
A program may use at most 64 MiB of HBM per device.

```python
import jax
import jax.numpy as jnp
from jax import lax

D = 8192
FF = 14336
TOKENS = 768


def shard_levels(own_key, dims, cuts, smallest, largest):
    gain, own = 1.0, jax.random.fold_in(own_key, 6)
    for position, parts in cuts:
        heights = jnp.exp(jax.random.uniform(jax.random.fold_in(own, position), (parts,), jnp.float32, smallest / len(cuts), largest / len(cuts)))
        gain = gain * jnp.repeat(heights, dims[position] // parts).reshape([-1 if axis == position else 1 for axis in range(len(dims))])
    return gain


def noise(key, dims, scale, reach, cuts=(), held_as=jnp.bfloat16):
    drawn = scale * jax.random.normal(key, dims, jnp.float32)
    if cuts:
        drawn = drawn * shard_levels(key, dims, cuts, -0.22, 0.18)
    return jnp.clip(drawn, -reach, reach).astype(held_as)


def setup_inputs(seed: int = 0) -> dict:
    splits = jax.random.split(jax.random.key(seed), 6)
    return {
        "tokens": noise(splits[0], (TOKENS, D), 1.0, 6.0, ((0, 32), (1, 16))),
        "out_grad": noise(splits[1], (TOKENS, D), 0.5, 3.0, ((0, 32), (1, 16))),
        "gate_weight": noise(splits[2], (D, FF), D ** -0.5, 0.0625, ((0, 16), (1, 32))),
        "up_weight": noise(splits[3], (D, FF), D ** -0.5, 0.0625, ((0, 16), (1, 32))),
        "down_weight": noise(splits[4], (FF, D), FF ** -0.5, 0.046875, ((0, 32), (1, 16))),
    }


def swiglu_grads(gate_value, up_value, hidden_grad):
    logistic = jax.nn.sigmoid(gate_value)
    swish = gate_value * logistic
    hidden = (swish * up_value).astype(jnp.bfloat16)
    up_delta = (hidden_grad * swish).astype(jnp.bfloat16)
    gate_delta = (hidden_grad * up_value * logistic * (1.0 + gate_value * (1.0 - logistic))).astype(jnp.bfloat16)
    return hidden, gate_delta, up_delta


def reference(tokens, out_grad, gate_weight, up_weight, down_weight):
    contract_last = (((1,), (1,)), ((), ()))
    contract_first = (((0,), (0,)), ((), ()))
    gate_value = jnp.dot(tokens, gate_weight, preferred_element_type=jnp.float32)
    up_value = jnp.dot(tokens, up_weight, preferred_element_type=jnp.float32)
    hidden_grad = lax.dot_general(out_grad, down_weight, contract_last, preferred_element_type=jnp.float32)
    hidden, gate_delta, up_delta = swiglu_grads(gate_value, up_value, hidden_grad)
    grad_down = lax.dot_general(hidden, out_grad, contract_first, preferred_element_type=jnp.float32).astype(jnp.bfloat16)
    grad_gate = lax.dot_general(tokens, gate_delta, contract_first, preferred_element_type=jnp.float32).astype(jnp.bfloat16)
    grad_up = lax.dot_general(tokens, up_delta, contract_first, preferred_element_type=jnp.float32).astype(jnp.bfloat16)
    grad_input = lax.dot_general(gate_delta, gate_weight, contract_last, preferred_element_type=jnp.float32)
    grad_input = grad_input + lax.dot_general(up_delta, up_weight, contract_last, preferred_element_type=jnp.float32)
    return grad_input.astype(jnp.bfloat16), grad_gate, grad_up, grad_down
```

```python
import jax
import jax.numpy as jnp
from jax import lax
from jax.sharding import Mesh, PartitionSpec as P


def swiglu_grads(gate_value, up_value, hidden_grad):
    logistic = jax.nn.sigmoid(gate_value)
    swish = gate_value * logistic
    hidden = (swish * up_value).astype(jnp.bfloat16)
    up_delta = (hidden_grad * swish).astype(jnp.bfloat16)
    gate_delta = (hidden_grad * up_value * logistic * (1.0 + gate_value * (1.0 - logistic))).astype(
        jnp.bfloat16
    )
    return (hidden, gate_delta, up_delta)


SEC = ("y", "zl", "c")
TEN = ("x", "zh")


def scatter_sum(v, axis_name, n, dim):
    shape = v.shape
    v = v.reshape(shape[:dim] + (n, shape[dim] // n) + shape[dim + 1 :])
    v = lax.all_to_all(v, axis_name, dim, dim, tiled=True)
    return v.sum(dim)


def local(tokens, out_grad, gate_weight, up_weight, down_weight, nx, nzh, nsec):
    contract_last = (((1,), (1,)), ((), ()))
    contract_first = (((0,), (0,)), ((), ()))
    all_tokens, all_grads = (
        lax.all_gather(tokens, SEC, axis=0, tiled=True),
        lax.all_gather(out_grad, SEC, axis=0, tiled=True),
    )
    gate_part = jnp.dot(all_tokens, gate_weight, preferred_element_type=jnp.float32)
    up_part = jnp.dot(all_tokens, up_weight, preferred_element_type=jnp.float32)
    hidden_part = lax.dot_general(
        all_grads, down_weight, contract_last, preferred_element_type=jnp.float32
    )
    parts = jnp.stack([gate_part, up_part, hidden_part])
    parts = scatter_sum(parts, "x", nx, 1)
    parts = scatter_sum(parts, "zh", nzh, 1)
    hidden, gate_delta, up_delta = swiglu_grads(parts[0], parts[1], parts[2])
    deltas = lax.all_gather(jnp.stack([hidden, gate_delta, up_delta]), TEN, axis=1, tiled=True)
    hidden, gate_delta, up_delta = deltas[0], deltas[1], deltas[2]
    grad_down = lax.dot_general(
        hidden, all_grads, contract_first, preferred_element_type=jnp.float32
    ).astype(jnp.bfloat16)
    grad_gate = lax.dot_general(
        all_tokens, gate_delta, contract_first, preferred_element_type=jnp.float32
    ).astype(jnp.bfloat16)
    grad_up = lax.dot_general(
        all_tokens, up_delta, contract_first, preferred_element_type=jnp.float32
    ).astype(jnp.bfloat16)
    result = lax.dot_general(
        gate_delta, gate_weight, contract_last, preferred_element_type=jnp.float32
    ) + lax.dot_general(up_delta, up_weight, contract_last, preferred_element_type=jnp.float32)
    grad_input = scatter_sum(result, SEC, nsec, 0).astype(jnp.bfloat16)
    return (grad_input, grad_gate, grad_up, grad_down)


def solution(mesh):
    nsec, nten = mesh.shape["section"], mesh.shape["tensor"]
    nzh = 4
    nx = nten // nzh
    fine = Mesh(mesh.devices.reshape(nsec // 4, 2, 2, nx, nzh), ("y", "zl", "c", "x", "zh"))
    act = P(SEC, TEN)
    wt = P(TEN, SEC)

    def body(*args):
        return local(*args, nx=nx, nzh=nzh, nsec=nsec)

    return jax.shard_map(
        body,
        mesh=fine,
        in_specs=(act, act, wt, wt, act),
        out_specs=(act, wt, wt, act),
        check_vma=False,
    )
```

```python
import jax
import jax.numpy as jnp
from jax import lax
from jax.sharding import Mesh, PartitionSpec as P


def swiglu_grads(gate_value, up_value, hidden_grad):
    logistic = jax.nn.sigmoid(gate_value)
    swish = gate_value * logistic
    hidden = (swish * up_value).astype(jnp.bfloat16)
    up_delta = (hidden_grad * swish).astype(jnp.bfloat16)
    gate_delta = (hidden_grad * up_value * logistic * (1.0 + gate_value * (1.0 - logistic))).astype(
        jnp.bfloat16
    )
    return (hidden, gate_delta, up_delta)


SEC = ("y", "zl", "c")
TEN = ("x", "zh")


def scatter_sum(v, axis_name, n, dim):
    shape = v.shape
    v = v.reshape(shape[:dim] + (n, shape[dim] // n) + shape[dim + 1 :])
    v = lax.all_to_all(v, axis_name, dim, dim, tiled=True)
    return v.sum(dim)


def gather_a2a(v, axis_name, n, dim):
    shape = v.shape
    v = jnp.broadcast_to(jnp.expand_dims(v, dim), shape[:dim] + (n,) + shape[dim:])
    v = lax.all_to_all(v, axis_name, dim, dim, tiled=True)
    return v.reshape(shape[:dim] + (n * shape[dim],) + shape[dim + 1 :])


def local(tokens, out_grad, gate_weight, up_weight, down_weight, nx, nzh, nsec):
    contract_last = (((1,), (1,)), ((), ()))
    contract_first = (((0,), (0,)), ((), ()))
    both = jnp.concatenate([tokens, out_grad], 1)
    both = gather_a2a(both, SEC, nsec, 0)
    all_tokens, all_grads = both[:, : tokens.shape[1]], both[:, tokens.shape[1] :]
    gate_part = jnp.dot(all_tokens, gate_weight, preferred_element_type=jnp.float32)
    up_part = jnp.dot(all_tokens, up_weight, preferred_element_type=jnp.float32)
    hidden_part = lax.dot_general(
        all_grads, down_weight, contract_last, preferred_element_type=jnp.float32
    )
    parts = jnp.stack([gate_part, up_part, hidden_part])
    parts = scatter_sum(parts, "x", nx, 1)
    parts = scatter_sum(parts, "zh", nzh, 1)
    hidden, gate_delta, up_delta = swiglu_grads(parts[0], parts[1], parts[2])
    deltas = jnp.stack([hidden, gate_delta, up_delta])
    deltas = gather_a2a(deltas, "zh", nzh, 1)
    deltas = gather_a2a(deltas, "x", nx, 1)
    hidden, gate_delta, up_delta = deltas[0], deltas[1], deltas[2]
    grad_down = lax.dot_general(
        hidden, all_grads, contract_first, preferred_element_type=jnp.float32
    ).astype(jnp.bfloat16)
    grad_gate = lax.dot_general(
        all_tokens, gate_delta, contract_first, preferred_element_type=jnp.float32
    ).astype(jnp.bfloat16)
    grad_up = lax.dot_general(
        all_tokens, up_delta, contract_first, preferred_element_type=jnp.float32
    ).astype(jnp.bfloat16)
    result = lax.dot_general(
        gate_delta, gate_weight, contract_last, preferred_element_type=jnp.float32
    ) + lax.dot_general(up_delta, up_weight, contract_last, preferred_element_type=jnp.float32)
    grad_input = scatter_sum(result, SEC, nsec, 0).astype(jnp.bfloat16)
    return (grad_input, grad_gate, grad_up, grad_down)


def solution(mesh):
    nsec, nten = mesh.shape["section"], mesh.shape["tensor"]
    nzh = 4
    nx = nten // nzh
    fine = Mesh(mesh.devices.reshape(nsec // 4, 2, 2, nx, nzh), ("y", "zl", "c", "x", "zh"))
    act = P(SEC, TEN)
    wt = P(TEN, SEC)

    def body(*args):
        return local(*args, nx=nx, nzh=nzh, nsec=nsec)

    return jax.shard_map(
        body,
        mesh=fine,
        in_specs=(act, act, wt, wt, act),
        out_specs=(act, wt, wt, act),
        check_vma=False,
    )
```

```python
import jax
import jax.numpy as jnp
from jax import lax
from jax.sharding import Mesh, PartitionSpec as P


def swiglu_grads(gate_value, up_value, hidden_grad):
    logistic = jax.nn.sigmoid(gate_value)
    swish = gate_value * logistic
    hidden = (swish * up_value).astype(jnp.bfloat16)
    up_delta = (hidden_grad * swish).astype(jnp.bfloat16)
    gate_delta = (hidden_grad * up_value * logistic * (1.0 + gate_value * (1.0 - logistic))).astype(
        jnp.bfloat16
    )
    return (hidden, gate_delta, up_delta)


SEC = ("y", "zl", "c")
TEN = ("x", "zh")


def scatter_sum(v, axis_name, n, dim):
    shape = v.shape
    v = v.reshape(shape[:dim] + (n, shape[dim] // n) + shape[dim + 1 :])
    v = lax.all_to_all(v, axis_name, dim, dim, tiled=True)
    return v.sum(dim)


def gather_a2a(v, axis_name, n, dim):
    shape = v.shape
    v = jnp.broadcast_to(jnp.expand_dims(v, dim), shape[:dim] + (n,) + shape[dim:])
    v = lax.all_to_all(v, axis_name, dim, dim, tiled=True)
    return v.reshape(shape[:dim] + (n * shape[dim],) + shape[dim + 1 :])


def local(tokens, out_grad, gate_weight, up_weight, down_weight, nx, nzh, nsec):
    contract_last = (((1,), (1,)), ((), ()))
    contract_first = (((0,), (0,)), ((), ()))
    all_tokens = gather_a2a(tokens, SEC, nsec, 0)
    all_grads = gather_a2a(out_grad, SEC, nsec, 0)
    gate_part = jnp.dot(all_tokens, gate_weight, preferred_element_type=jnp.float32)
    up_part = jnp.dot(all_tokens, up_weight, preferred_element_type=jnp.float32)
    hidden_part = lax.dot_general(
        all_grads, down_weight, contract_last, preferred_element_type=jnp.float32
    )
    gu = scatter_sum(jnp.stack([gate_part, up_part]), "x", nx, 1)
    hg = scatter_sum(hidden_part, "x", nx, 0)
    gu = scatter_sum(gu, "zh", nzh, 1)
    hg = scatter_sum(hg, "zh", nzh, 0)
    hidden, gate_delta, up_delta = swiglu_grads(gu[0], gu[1], hg)
    deltas = jnp.stack([hidden, gate_delta, up_delta])
    deltas = gather_a2a(deltas, "zh", nzh, 1)
    deltas = gather_a2a(deltas, "x", nx, 1)
    hidden, gate_delta, up_delta = deltas[0], deltas[1], deltas[2]
    grad_down = lax.dot_general(
        hidden, all_grads, contract_first, preferred_element_type=jnp.float32
    ).astype(jnp.bfloat16)
    grad_gate = lax.dot_general(
        all_tokens, gate_delta, contract_first, preferred_element_type=jnp.float32
    ).astype(jnp.bfloat16)
    grad_up = lax.dot_general(
        all_tokens, up_delta, contract_first, preferred_element_type=jnp.float32
    ).astype(jnp.bfloat16)
    result = lax.dot_general(
        gate_delta, gate_weight, contract_last, preferred_element_type=jnp.float32
    ) + lax.dot_general(up_delta, up_weight, contract_last, preferred_element_type=jnp.float32)
    grad_input = scatter_sum(result, SEC, nsec, 0).astype(jnp.bfloat16)
    return (grad_input, grad_gate, grad_up, grad_down)


def solution(mesh):
    nsec, nten = mesh.shape["section"], mesh.shape["tensor"]
    nzh = 4
    nx = nten // nzh
    fine = Mesh(mesh.devices.reshape(nsec // 4, 2, 2, nx, nzh), ("y", "zl", "c", "x", "zh"))
    act = P(SEC, TEN)
    wt = P(TEN, SEC)

    def body(*args):
        return local(*args, nx=nx, nzh=nzh, nsec=nsec)

    return jax.shard_map(
        body,
        mesh=fine,
        in_specs=(act, act, wt, wt, act),
        out_specs=(act, wt, wt, act),
        check_vma=False,
    )
```

```python
import jax
import jax.numpy as jnp
from jax import lax
from jax.sharding import Mesh, PartitionSpec as P


def swiglu_grads(gate_value, up_value, hidden_grad):
    logistic = jax.nn.sigmoid(gate_value)
    swish = gate_value * logistic
    hidden = (swish * up_value).astype(jnp.bfloat16)
    up_delta = (hidden_grad * swish).astype(jnp.bfloat16)
    gate_delta = (hidden_grad * up_value * logistic * (1.0 + gate_value * (1.0 - logistic))).astype(
        jnp.bfloat16
    )
    return (hidden, gate_delta, up_delta)


SEC = ("y", "zl", "c")
TEN = ("x", "zh")


def scatter_sum(v, axis_name, n, dim):
    shape = v.shape
    v = v.reshape(shape[:dim] + (n, shape[dim] // n) + shape[dim + 1 :])
    v = lax.all_to_all(v, axis_name, dim, dim, tiled=True)
    return v.sum(dim)


def gather_a2a(v, axis_name, n, dim):
    shape = v.shape
    v = jnp.broadcast_to(jnp.expand_dims(v, dim), shape[:dim] + (n,) + shape[dim:])
    v = lax.all_to_all(v, axis_name, dim, dim, tiled=True)
    return v.reshape(shape[:dim] + (n * shape[dim],) + shape[dim + 1 :])


def local(tokens, out_grad, gate_weight, up_weight, down_weight, nx, nzh, nsec):
    contract_last = (((1,), (1,)), ((), ()))
    contract_first = (((0,), (0,)), ((), ()))
    both = jnp.concatenate([tokens, out_grad], 1)
    both = gather_a2a(both, ("y", "zl"), nsec // 2, 0)
    both = both.reshape((nsec // 2, 1, -1) + both.shape[1:])
    both = gather_a2a(both, "c", 2, 1).reshape((-1,) + both.shape[3:])
    all_tokens, all_grads = both[:, : tokens.shape[1]], both[:, tokens.shape[1] :]
    gate_part = jnp.dot(all_tokens, gate_weight, preferred_element_type=jnp.float32)
    up_part = jnp.dot(all_tokens, up_weight, preferred_element_type=jnp.float32)
    hidden_part = lax.dot_general(
        all_grads, down_weight, contract_last, preferred_element_type=jnp.float32
    )
    parts = jnp.stack([gate_part, up_part, hidden_part])
    parts = scatter_sum(parts, "x", nx, 1)
    parts = scatter_sum(parts, "zh", nzh, 1)
    hidden, gate_delta, up_delta = swiglu_grads(parts[0], parts[1], parts[2])
    deltas = jnp.stack([hidden, gate_delta, up_delta])
    deltas = gather_a2a(deltas, "zh", nzh, 1)
    deltas = gather_a2a(deltas, "x", nx, 1)
    hidden, gate_delta, up_delta = deltas[0], deltas[1], deltas[2]
    grad_down = lax.dot_general(
        hidden, all_grads, contract_first, preferred_element_type=jnp.float32
    ).astype(jnp.bfloat16)
    grad_gate = lax.dot_general(
        all_tokens, gate_delta, contract_first, preferred_element_type=jnp.float32
    ).astype(jnp.bfloat16)
    grad_up = lax.dot_general(
        all_tokens, up_delta, contract_first, preferred_element_type=jnp.float32
    ).astype(jnp.bfloat16)
    result = lax.dot_general(
        gate_delta, gate_weight, contract_last, preferred_element_type=jnp.float32
    ) + lax.dot_general(up_delta, up_weight, contract_last, preferred_element_type=jnp.float32)
    result = result.reshape((nsec // 2, 2, -1) + result.shape[1:])
    result = scatter_sum(result, "c", 2, 1).reshape((-1,) + result.shape[3:])
    grad_input = scatter_sum(result, ("y", "zl"), nsec // 2, 0).astype(jnp.bfloat16)
    return (grad_input, grad_gate, grad_up, grad_down)


def solution(mesh):
    nsec, nten = mesh.shape["section"], mesh.shape["tensor"]
    nzh = 4
    nx = nten // nzh
    fine = Mesh(mesh.devices.reshape(nsec // 4, 2, 2, nx, nzh), ("y", "zl", "c", "x", "zh"))
    act = P(SEC, TEN)
    wt = P(TEN, SEC)

    def body(*args):
        return local(*args, nx=nx, nzh=nzh, nsec=nsec)

    return jax.shard_map(
        body,
        mesh=fine,
        in_specs=(act, act, wt, wt, act),
        out_specs=(act, wt, wt, act),
        check_vma=False,
    )
```

```python
import jax
import jax.numpy as jnp
from jax import lax
from jax.sharding import Mesh, PartitionSpec as P


def swiglu_grads(gate_value, up_value, hidden_grad):
    logistic = jax.nn.sigmoid(gate_value)
    swish = gate_value * logistic
    hidden = (swish * up_value).astype(jnp.bfloat16)
    up_delta = (hidden_grad * swish).astype(jnp.bfloat16)
    gate_delta = (hidden_grad * up_value * logistic * (1.0 + gate_value * (1.0 - logistic))).astype(
        jnp.bfloat16
    )
    return (hidden, gate_delta, up_delta)


SEC = ("y", "zl", "c")
TEN = ("x", "zh")


def scatter_sum(v, axis_name, n, dim):
    shape = v.shape
    v = v.reshape(shape[:dim] + (n, shape[dim] // n) + shape[dim + 1 :])
    v = lax.all_to_all(v, axis_name, dim, dim, tiled=True)
    return v.sum(dim)


def gather_a2a(v, axis_name, n, dim):
    shape = v.shape
    v = jnp.broadcast_to(jnp.expand_dims(v, dim), shape[:dim] + (n,) + shape[dim:])
    v = lax.all_to_all(v, axis_name, dim, dim, tiled=True)
    return v.reshape(shape[:dim] + (n * shape[dim],) + shape[dim + 1 :])


def local(tokens, out_grad, gate_weight, up_weight, down_weight, nx, nzh, nsec):
    contract_last = (((1,), (1,)), ((), ()))
    contract_first = (((0,), (0,)), ((), ()))
    both = jnp.concatenate([tokens, out_grad], 1)
    both = gather_a2a(both, ("y", "zl"), nsec // 2, 0)
    both = both.reshape((nsec // 2, 1, -1) + both.shape[1:])
    both = gather_a2a(both, "c", 2, 1).reshape((-1,) + both.shape[3:])
    all_tokens, all_grads = both[:, : tokens.shape[1]], both[:, tokens.shape[1] :]
    gate_part = jnp.dot(all_tokens, gate_weight, preferred_element_type=jnp.float32)
    up_part = jnp.dot(all_tokens, up_weight, preferred_element_type=jnp.float32)
    hidden_part = lax.dot_general(
        all_grads, down_weight, contract_last, preferred_element_type=jnp.float32
    )
    parts = jnp.stack([gate_part, up_part, hidden_part])
    width = parts.shape[2] // 2
    chunks = []
    for c in range(2):
        p = parts[:, :, c * width : (c + 1) * width]
        p = scatter_sum(p, "x", nx, 1)
        p = lax.psum_scatter(p, "zh", scatter_dimension=1, tiled=True)
        d = jnp.stack(swiglu_grads(p[0], p[1], p[2]))
        d = lax.all_gather(d, "zh", axis=1, tiled=True)
        chunks.append(gather_a2a(d, "x", nx, 1))
    deltas = jnp.concatenate(chunks, 2)
    hidden, gate_delta, up_delta = deltas[0], deltas[1], deltas[2]
    grad_down = lax.dot_general(
        hidden, all_grads, contract_first, preferred_element_type=jnp.float32
    ).astype(jnp.bfloat16)
    grad_gate = lax.dot_general(
        all_tokens, gate_delta, contract_first, preferred_element_type=jnp.float32
    ).astype(jnp.bfloat16)
    grad_up = lax.dot_general(
        all_tokens, up_delta, contract_first, preferred_element_type=jnp.float32
    ).astype(jnp.bfloat16)
    result = lax.dot_general(
        gate_delta, gate_weight, contract_last, preferred_element_type=jnp.float32
    ) + lax.dot_general(up_delta, up_weight, contract_last, preferred_element_type=jnp.float32)
    result = result.reshape((nsec // 2, 2, -1) + result.shape[1:])
    result = scatter_sum(result, "c", 2, 1).reshape((-1,) + result.shape[3:])
    grad_input = scatter_sum(result, ("y", "zl"), nsec // 2, 0).astype(jnp.bfloat16)
    return (grad_input, grad_gate, grad_up, grad_down)


def solution(mesh):
    nsec, nten = mesh.shape["section"], mesh.shape["tensor"]
    nzh = 4
    nx = nten // nzh
    fine = Mesh(mesh.devices.reshape(nsec // 4, 2, 2, nx, nzh), ("y", "zl", "c", "x", "zh"))
    act = P(SEC, TEN)
    wt = P(TEN, SEC)

    def body(*args):
        return local(*args, nx=nx, nzh=nzh, nsec=nsec)

    return jax.shard_map(
        body,
        mesh=fine,
        in_specs=(act, act, wt, wt, act),
        out_specs=(act, wt, wt, act),
        check_vma=False,
    )
```

```python
import jax
import jax.numpy as jnp
from jax import lax
from jax.sharding import Mesh, PartitionSpec as P


def swiglu_grads(gate_value, up_value, hidden_grad):
    logistic = jax.nn.sigmoid(gate_value)
    swish = gate_value * logistic
    hidden = (swish * up_value).astype(jnp.bfloat16)
    up_delta = (hidden_grad * swish).astype(jnp.bfloat16)
    gate_delta = (hidden_grad * up_value * logistic * (1.0 + gate_value * (1.0 - logistic))).astype(
        jnp.bfloat16
    )
    return (hidden, gate_delta, up_delta)


SEC = ("y", "zl", "c")
TEN = ("x", "zh")


def scatter_sum(v, axis_name, n, dim):
    shape = v.shape
    v = v.reshape(shape[:dim] + (n, shape[dim] // n) + shape[dim + 1 :])
    v = lax.all_to_all(v, axis_name, dim, dim, tiled=True)
    return v.sum(dim)


def gather_a2a(v, axis_name, n, dim):
    shape = v.shape
    v = jnp.broadcast_to(jnp.expand_dims(v, dim), shape[:dim] + (n,) + shape[dim:])
    v = lax.all_to_all(v, axis_name, dim, dim, tiled=True)
    return v.reshape(shape[:dim] + (n * shape[dim],) + shape[dim + 1 :])


def scatter_permute(v, axis_name, n, dim):
    me = lax.axis_index(axis_name)
    shape = v.shape
    size = shape[dim] // n
    total = lax.dynamic_slice_in_dim(v, me * size, size, dim)
    for k in range(1, n):
        part = lax.dynamic_slice_in_dim(v, ((me + k) % n) * size, size, dim)
        total = total + lax.ppermute(part, axis_name, [(j, (j + k) % n) for j in range(n)])
    return total


def gather_permute(v, axis_name, n, dim):
    me = lax.axis_index(axis_name)
    got = [v] + [
        lax.ppermute(v, axis_name, [(j, (j + k) % n) for j in range(n)]) for k in range(1, n)
    ]
    ordered = jnp.stack([got[0]] + got[:0:-1])
    ordered = jnp.roll(ordered, me, axis=0)
    ordered = jnp.moveaxis(ordered, 0, dim)
    shape = v.shape
    return ordered.reshape(shape[:dim] + (n * shape[dim],) + shape[dim + 1 :])


def local(tokens, out_grad, gate_weight, up_weight, down_weight, nx, nzh, nsec):
    contract_last = (((1,), (1,)), ((), ()))
    contract_first = (((0,), (0,)), ((), ()))
    both = jnp.concatenate([tokens, out_grad], 1)
    both = gather_a2a(both, ("y", "zl"), nsec // 2, 0)
    both = both.reshape((nsec // 2, 1, -1) + both.shape[1:])
    both = gather_a2a(both, "c", 2, 1).reshape((-1,) + both.shape[3:])
    all_tokens, all_grads = both[:, : tokens.shape[1]], both[:, tokens.shape[1] :]
    rows = all_tokens.shape[0] // 2
    chunks = []
    for c in range(2):
        tok = all_tokens[c * rows : (c + 1) * rows]
        grd = all_grads[c * rows : (c + 1) * rows]
        gate_part = jnp.dot(tok, gate_weight, preferred_element_type=jnp.float32)
        up_part = jnp.dot(tok, up_weight, preferred_element_type=jnp.float32)
        hidden_part = lax.dot_general(
            grd, down_weight, contract_last, preferred_element_type=jnp.float32
        )
        p = jnp.stack([gate_part, up_part, hidden_part])
        p = scatter_sum(p, "x", nx, 1)
        p = scatter_permute(p, "zh", nzh, 1)
        d = jnp.stack(swiglu_grads(p[0], p[1], p[2]))
        d = gather_permute(d, "zh", nzh, 1)
        chunks.append(gather_a2a(d, "x", nx, 1))
    deltas = jnp.concatenate(chunks, 1)
    hidden, gate_delta, up_delta = deltas[0], deltas[1], deltas[2]
    grad_down = lax.dot_general(
        hidden, all_grads, contract_first, preferred_element_type=jnp.float32
    ).astype(jnp.bfloat16)
    grad_gate = lax.dot_general(
        all_tokens, gate_delta, contract_first, preferred_element_type=jnp.float32
    ).astype(jnp.bfloat16)
    grad_up = lax.dot_general(
        all_tokens, up_delta, contract_first, preferred_element_type=jnp.float32
    ).astype(jnp.bfloat16)
    result = lax.dot_general(
        gate_delta, gate_weight, contract_last, preferred_element_type=jnp.float32
    ) + lax.dot_general(up_delta, up_weight, contract_last, preferred_element_type=jnp.float32)
    result = result.reshape((nsec // 2, 2, -1) + result.shape[1:])
    result = scatter_sum(result, "c", 2, 1).reshape((-1,) + result.shape[3:])
    grad_input = scatter_sum(result, ("y", "zl"), nsec // 2, 0).astype(jnp.bfloat16)
    return (grad_input, grad_gate, grad_up, grad_down)


def solution(mesh):
    nsec, nten = mesh.shape["section"], mesh.shape["tensor"]
    nzh = 4
    nx = nten // nzh
    fine = Mesh(mesh.devices.reshape(nsec // 4, 2, 2, nx, nzh), ("y", "zl", "c", "x", "zh"))
    act = P(SEC, TEN)
    wt = P(TEN, SEC)

    def body(*args):
        return local(*args, nx=nx, nzh=nzh, nsec=nsec)

    return jax.shard_map(
        body,
        mesh=fine,
        in_specs=(act, act, wt, wt, act),
        out_specs=(act, wt, wt, act),
        check_vma=False,
    )
```

```python
import jax
import jax.numpy as jnp
from jax import lax
from jax.sharding import Mesh, PartitionSpec as P


def swiglu_grads(gate_value, up_value, hidden_grad):
    logistic = jax.nn.sigmoid(gate_value)
    swish = gate_value * logistic
    hidden = (swish * up_value).astype(jnp.bfloat16)
    up_delta = (hidden_grad * swish).astype(jnp.bfloat16)
    gate_delta = (hidden_grad * up_value * logistic * (1.0 + gate_value * (1.0 - logistic))).astype(
        jnp.bfloat16
    )
    return (hidden, gate_delta, up_delta)


SEC = ("y", "zl", "c")
TEN = ("x", "zh")


def scatter_sum(v, axis_name, n, dim):
    shape = v.shape
    v = v.reshape(shape[:dim] + (n, shape[dim] // n) + shape[dim + 1 :])
    v = lax.all_to_all(v, axis_name, dim, dim, tiled=True)
    return v.sum(dim)


def gather_a2a(v, axis_name, n, dim):
    shape = v.shape
    v = jnp.broadcast_to(jnp.expand_dims(v, dim), shape[:dim] + (n,) + shape[dim:])
    v = lax.all_to_all(v, axis_name, dim, dim, tiled=True)
    return v.reshape(shape[:dim] + (n * shape[dim],) + shape[dim + 1 :])


def scatter_permute(v, axis_name, n, dim):
    me = lax.axis_index(axis_name)
    shape = v.shape
    size = shape[dim] // n
    total = lax.dynamic_slice_in_dim(v, me * size, size, dim)
    for k in range(1, n):
        part = lax.dynamic_slice_in_dim(v, ((me + k) % n) * size, size, dim)
        total = total + lax.ppermute(part, axis_name, [(j, (j + k) % n) for j in range(n)])
    return total


def gather_permute(v, axis_name, n, dim):
    me = lax.axis_index(axis_name)
    got = [v] + [
        lax.ppermute(v, axis_name, [(j, (j + k) % n) for j in range(n)]) for k in range(1, n)
    ]
    ordered = jnp.stack([got[0]] + got[:0:-1])
    ordered = jnp.roll(ordered, me, axis=0)
    ordered = jnp.moveaxis(ordered, 0, dim)
    shape = v.shape
    return ordered.reshape(shape[:dim] + (n * shape[dim],) + shape[dim + 1 :])


def local(tokens, out_grad, gate_weight, up_weight, down_weight, nx, nzh, nsec):
    contract_last = (((1,), (1,)), ((), ()))
    contract_first = (((0,), (0,)), ((), ()))
    both = jnp.concatenate([tokens, out_grad], 1)
    both = gather_a2a(both, ("y", "zl"), nsec // 2, 0)
    both = both.reshape((nsec // 2, 1, -1) + both.shape[1:])
    both = gather_a2a(both, "c", 2, 1).reshape((-1,) + both.shape[3:])
    all_tokens, all_grads = both[:, : tokens.shape[1]], both[:, tokens.shape[1] :]
    rows = all_tokens.shape[0] // 2
    chunks = []
    for c in range(2):
        tok = all_tokens[c * rows : (c + 1) * rows]
        grd = all_grads[c * rows : (c + 1) * rows]
        gate_part = jnp.dot(tok, gate_weight, preferred_element_type=jnp.float32)
        up_part = jnp.dot(tok, up_weight, preferred_element_type=jnp.float32)
        hidden_part = lax.dot_general(
            grd, down_weight, contract_last, preferred_element_type=jnp.float32
        )
        p = jnp.stack([gate_part, up_part, hidden_part])
        p = scatter_sum(p, "x", nx, 1)
        p = scatter_permute(p, "zh", nzh, 1)
        d = jnp.stack(swiglu_grads(p[0], p[1], p[2]))
        d = gather_a2a(d, "zh", nzh, 1)
        chunks.append(gather_a2a(d, "x", nx, 1))
    deltas = jnp.concatenate(chunks, 1)
    hidden, gate_delta, up_delta = deltas[0], deltas[1], deltas[2]
    grad_down = lax.dot_general(
        hidden, all_grads, contract_first, preferred_element_type=jnp.float32
    ).astype(jnp.bfloat16)
    grad_gate = lax.dot_general(
        all_tokens, gate_delta, contract_first, preferred_element_type=jnp.float32
    ).astype(jnp.bfloat16)
    grad_up = lax.dot_general(
        all_tokens, up_delta, contract_first, preferred_element_type=jnp.float32
    ).astype(jnp.bfloat16)
    result = lax.dot_general(
        gate_delta, gate_weight, contract_last, preferred_element_type=jnp.float32
    ) + lax.dot_general(up_delta, up_weight, contract_last, preferred_element_type=jnp.float32)
    result = result.reshape((nsec // 2, 2, -1) + result.shape[1:])
    result = scatter_sum(result, "c", 2, 1).reshape((-1,) + result.shape[3:])
    grad_input = scatter_sum(result, ("y", "zl"), nsec // 2, 0).astype(jnp.bfloat16)
    return (grad_input, grad_gate, grad_up, grad_down)


def solution(mesh):
    nsec, nten = mesh.shape["section"], mesh.shape["tensor"]
    nzh = 4
    nx = nten // nzh
    fine = Mesh(mesh.devices.reshape(nsec // 4, 2, 2, nx, nzh), ("y", "zl", "c", "x", "zh"))
    act = P(SEC, TEN)
    wt = P(TEN, SEC)

    def body(*args):
        return local(*args, nx=nx, nzh=nzh, nsec=nsec)

    return jax.shard_map(
        body,
        mesh=fine,
        in_specs=(act, act, wt, wt, act),
        out_specs=(act, wt, wt, act),
        check_vma=False,
    )
```

```python
import jax
import jax.numpy as jnp
from jax import lax
from jax.sharding import Mesh, PartitionSpec as P


def swiglu_grads(gate_value, up_value, hidden_grad):
    logistic = jax.nn.sigmoid(gate_value)
    swish = gate_value * logistic
    hidden = (swish * up_value).astype(jnp.bfloat16)
    up_delta = (hidden_grad * swish).astype(jnp.bfloat16)
    gate_delta = (hidden_grad * up_value * logistic * (1.0 + gate_value * (1.0 - logistic))).astype(
        jnp.bfloat16
    )
    return (hidden, gate_delta, up_delta)


SEC = ("y", "zl", "c")
TEN = ("x", "zh")


def scatter_sum(v, axis_name, n, dim):
    shape = v.shape
    v = v.reshape(shape[:dim] + (n, shape[dim] // n) + shape[dim + 1 :])
    v = lax.all_to_all(v, axis_name, dim, dim, tiled=True)
    return v.sum(dim)


def gather_a2a(v, axis_name, n, dim):
    shape = v.shape
    v = jnp.broadcast_to(jnp.expand_dims(v, dim), shape[:dim] + (n,) + shape[dim:])
    v = lax.all_to_all(v, axis_name, dim, dim, tiled=True)
    return v.reshape(shape[:dim] + (n * shape[dim],) + shape[dim + 1 :])


def scatter_permute(v, axis_name, n, dim):
    me = lax.axis_index(axis_name)
    shape = v.shape
    size = shape[dim] // n
    total = lax.dynamic_slice_in_dim(v, me * size, size, dim)
    for k in range(1, n):
        part = lax.dynamic_slice_in_dim(v, ((me + k) % n) * size, size, dim)
        total = total + lax.ppermute(part, axis_name, [(j, (j + k) % n) for j in range(n)])
    return total


def gather_permute(v, axis_name, n, dim):
    me = lax.axis_index(axis_name)
    got = [v] + [
        lax.ppermute(v, axis_name, [(j, (j + k) % n) for j in range(n)]) for k in range(1, n)
    ]
    ordered = jnp.stack([got[0]] + got[:0:-1])
    ordered = jnp.roll(ordered, me, axis=0)
    ordered = jnp.moveaxis(ordered, 0, dim)
    shape = v.shape
    return ordered.reshape(shape[:dim] + (n * shape[dim],) + shape[dim + 1 :])


def local(tokens, out_grad, gate_weight, up_weight, down_weight, nx, nzh, nsec):
    contract_last = (((1,), (1,)), ((), ()))
    contract_first = (((0,), (0,)), ((), ()))
    both = jnp.concatenate([tokens, out_grad], 1)
    both = gather_a2a(both, ("y", "zl"), nsec // 2, 0)
    both = both.reshape((nsec // 2, 1, -1) + both.shape[1:])
    both = gather_a2a(both, "c", 2, 1).reshape((-1,) + both.shape[3:])
    all_tokens, all_grads = both[:, : tokens.shape[1]], both[:, tokens.shape[1] :]
    rows = all_tokens.shape[0] // 2
    chunks = []
    for c in range(2):
        tok = all_tokens[c * rows : (c + 1) * rows]
        grd = all_grads[c * rows : (c + 1) * rows]
        gate_part = jnp.dot(tok, gate_weight, preferred_element_type=jnp.float32)
        up_part = jnp.dot(tok, up_weight, preferred_element_type=jnp.float32)
        hidden_part = lax.dot_general(
            grd, down_weight, contract_last, preferred_element_type=jnp.float32
        )
        p = jnp.stack([gate_part, up_part, hidden_part])
        p = scatter_sum(p, "x", nx, 1)
        p = scatter_permute(p, "zh", nzh, 1)
        d = jnp.stack(swiglu_grads(p[0], p[1], p[2]))
        d = gather_permute(d, "zh", nzh, 1)
        chunks.append(gather_permute(d, "x", nx, 1))
    deltas = jnp.concatenate(chunks, 1)
    hidden, gate_delta, up_delta = deltas[0], deltas[1], deltas[2]
    grad_down = lax.dot_general(
        hidden, all_grads, contract_first, preferred_element_type=jnp.float32
    ).astype(jnp.bfloat16)
    grad_gate = lax.dot_general(
        all_tokens, gate_delta, contract_first, preferred_element_type=jnp.float32
    ).astype(jnp.bfloat16)
    grad_up = lax.dot_general(
        all_tokens, up_delta, contract_first, preferred_element_type=jnp.float32
    ).astype(jnp.bfloat16)
    result = lax.dot_general(
        gate_delta, gate_weight, contract_last, preferred_element_type=jnp.float32
    ) + lax.dot_general(up_delta, up_weight, contract_last, preferred_element_type=jnp.float32)
    result = result.reshape((nsec // 2, 2, -1) + result.shape[1:])
    result = scatter_sum(result, "c", 2, 1).reshape((-1,) + result.shape[3:])
    grad_input = scatter_sum(result, ("y", "zl"), nsec // 2, 0).astype(jnp.bfloat16)
    return (grad_input, grad_gate, grad_up, grad_down)


def solution(mesh):
    nsec, nten = mesh.shape["section"], mesh.shape["tensor"]
    nzh = 4
    nx = nten // nzh
    fine = Mesh(mesh.devices.reshape(nsec // 4, 2, 2, nx, nzh), ("y", "zl", "c", "x", "zh"))
    act = P(SEC, TEN)
    wt = P(TEN, SEC)

    def body(*args):
        return local(*args, nx=nx, nzh=nzh, nsec=nsec)

    return jax.shard_map(
        body,
        mesh=fine,
        in_specs=(act, act, wt, wt, act),
        out_specs=(act, wt, wt, act),
        check_vma=False,
    )
```

```python
import jax
import jax.numpy as jnp
from jax import lax
from jax.sharding import Mesh, PartitionSpec as P


def swiglu_grads(gate_value, up_value, hidden_grad):
    logistic = jax.nn.sigmoid(gate_value)
    swish = gate_value * logistic
    hidden = (swish * up_value).astype(jnp.bfloat16)
    up_delta = (hidden_grad * swish).astype(jnp.bfloat16)
    gate_delta = (hidden_grad * up_value * logistic * (1.0 + gate_value * (1.0 - logistic))).astype(
        jnp.bfloat16
    )
    return (hidden, gate_delta, up_delta)


SEC = ("y", "zl", "c")
TEN = ("x", "zh")


def scatter_sum(v, axis_name, n, dim):
    shape = v.shape
    v = v.reshape(shape[:dim] + (n, shape[dim] // n) + shape[dim + 1 :])
    v = lax.all_to_all(v, axis_name, dim, dim, tiled=True)
    return v.sum(dim)


def gather_a2a(v, axis_name, n, dim):
    shape = v.shape
    v = jnp.broadcast_to(jnp.expand_dims(v, dim), shape[:dim] + (n,) + shape[dim:])
    v = lax.all_to_all(v, axis_name, dim, dim, tiled=True)
    return v.reshape(shape[:dim] + (n * shape[dim],) + shape[dim + 1 :])


def scatter_permute(v, axis_name, n, dim):
    me = lax.axis_index(axis_name)
    shape = v.shape
    size = shape[dim] // n
    total = lax.dynamic_slice_in_dim(v, me * size, size, dim)
    for k in range(1, n):
        part = lax.dynamic_slice_in_dim(v, ((me + k) % n) * size, size, dim)
        total = total + lax.ppermute(part, axis_name, [(j, (j + k) % n) for j in range(n)])
    return total


def gather_permute(v, axis_name, n, dim):
    me = lax.axis_index(axis_name)
    got = [v] + [
        lax.ppermute(v, axis_name, [(j, (j + k) % n) for j in range(n)]) for k in range(1, n)
    ]
    ordered = jnp.stack([got[0]] + got[:0:-1])
    ordered = jnp.roll(ordered, me, axis=0)
    ordered = jnp.moveaxis(ordered, 0, dim)
    shape = v.shape
    return ordered.reshape(shape[:dim] + (n * shape[dim],) + shape[dim + 1 :])


def local(tokens, out_grad, gate_weight, up_weight, down_weight, nx, nzh, nsec):
    contract_last = (((1,), (1,)), ((), ()))
    contract_first = (((0,), (0,)), ((), ()))
    both = jnp.concatenate([tokens, out_grad], 1)
    both = gather_a2a(both, ("y", "zl"), nsec // 2, 0)
    both = both.reshape((nsec // 2, 1, -1) + both.shape[1:])
    both = gather_a2a(both, "c", 2, 1).reshape((-1,) + both.shape[3:])
    all_tokens, all_grads = both[:, : tokens.shape[1]], both[:, tokens.shape[1] :]
    nchunk = 3
    rows = all_tokens.shape[0] // nchunk
    chunks = []
    for c in range(nchunk):
        tok = all_tokens[c * rows : (c + 1) * rows]
        grd = all_grads[c * rows : (c + 1) * rows]
        gate_part = jnp.dot(tok, gate_weight, preferred_element_type=jnp.float32)
        up_part = jnp.dot(tok, up_weight, preferred_element_type=jnp.float32)
        hidden_part = lax.dot_general(
            grd, down_weight, contract_last, preferred_element_type=jnp.float32
        )
        p = jnp.stack([gate_part, up_part, hidden_part])
        p = scatter_sum(p, "x", nx, 1)
        p = scatter_permute(p, "zh", nzh, 1)
        d = jnp.stack(swiglu_grads(p[0], p[1], p[2]))
        d = gather_permute(d, "zh", nzh, 1)
        chunks.append(gather_a2a(d, "x", nx, 1))
    deltas = jnp.concatenate(chunks, 1)
    hidden, gate_delta, up_delta = deltas[0], deltas[1], deltas[2]
    grad_down = lax.dot_general(
        hidden, all_grads, contract_first, preferred_element_type=jnp.float32
    ).astype(jnp.bfloat16)
    grad_gate = lax.dot_general(
        all_tokens, gate_delta, contract_first, preferred_element_type=jnp.float32
    ).astype(jnp.bfloat16)
    grad_up = lax.dot_general(
        all_tokens, up_delta, contract_first, preferred_element_type=jnp.float32
    ).astype(jnp.bfloat16)
    result = lax.dot_general(
        gate_delta, gate_weight, contract_last, preferred_element_type=jnp.float32
    ) + lax.dot_general(up_delta, up_weight, contract_last, preferred_element_type=jnp.float32)
    result = result.reshape((nsec // 2, 2, -1) + result.shape[1:])
    result = scatter_sum(result, "c", 2, 1).reshape((-1,) + result.shape[3:])
    grad_input = scatter_sum(result, ("y", "zl"), nsec // 2, 0).astype(jnp.bfloat16)
    return (grad_input, grad_gate, grad_up, grad_down)


def solution(mesh):
    nsec, nten = mesh.shape["section"], mesh.shape["tensor"]
    nzh = 4
    nx = nten // nzh
    fine = Mesh(mesh.devices.reshape(nsec // 4, 2, 2, nx, nzh), ("y", "zl", "c", "x", "zh"))
    act = P(SEC, TEN)
    wt = P(TEN, SEC)

    def body(*args):
        return local(*args, nx=nx, nzh=nzh, nsec=nsec)

    return jax.shard_map(
        body,
        mesh=fine,
        in_specs=(act, act, wt, wt, act),
        out_specs=(act, wt, wt, act),
        check_vma=False,
    )
```

```python
import jax
import jax.numpy as jnp
from jax import lax
from jax.sharding import Mesh, PartitionSpec as P


def swiglu_grads(gate_value, up_value, hidden_grad):
    logistic = jax.nn.sigmoid(gate_value)
    swish = gate_value * logistic
    hidden = (swish * up_value).astype(jnp.bfloat16)
    up_delta = (hidden_grad * swish).astype(jnp.bfloat16)
    gate_delta = (hidden_grad * up_value * logistic * (1.0 + gate_value * (1.0 - logistic))).astype(
        jnp.bfloat16
    )
    return (hidden, gate_delta, up_delta)


SEC = ("y", "zl", "c")
TEN = ("x", "zh")


def scatter_sum(v, axis_name, n, dim):
    shape = v.shape
    v = v.reshape(shape[:dim] + (n, shape[dim] // n) + shape[dim + 1 :])
    v = lax.all_to_all(v, axis_name, dim, dim, tiled=True)
    return v.sum(dim)


def gather_a2a(v, axis_name, n, dim):
    shape = v.shape
    v = jnp.broadcast_to(jnp.expand_dims(v, dim), shape[:dim] + (n,) + shape[dim:])
    v = lax.all_to_all(v, axis_name, dim, dim, tiled=True)
    return v.reshape(shape[:dim] + (n * shape[dim],) + shape[dim + 1 :])


def scatter_permute(v, axis_name, n, dim):
    me = lax.axis_index(axis_name)
    shape = v.shape
    size = shape[dim] // n
    total = lax.dynamic_slice_in_dim(v, me * size, size, dim)
    for k in range(1, n):
        part = lax.dynamic_slice_in_dim(v, ((me + k) % n) * size, size, dim)
        total = total + lax.ppermute(part, axis_name, [(j, (j + k) % n) for j in range(n)])
    return total


def gather_permute(v, axis_name, n, dim):
    me = lax.axis_index(axis_name)
    got = [v] + [
        lax.ppermute(v, axis_name, [(j, (j + k) % n) for j in range(n)]) for k in range(1, n)
    ]
    ordered = jnp.stack([got[0]] + got[:0:-1])
    ordered = jnp.roll(ordered, me, axis=0)
    ordered = jnp.moveaxis(ordered, 0, dim)
    shape = v.shape
    return ordered.reshape(shape[:dim] + (n * shape[dim],) + shape[dim + 1 :])


def local(tokens, out_grad, gate_weight, up_weight, down_weight, nx, nzh, nsec):
    contract_last = (((1,), (1,)), ((), ()))
    contract_first = (((0,), (0,)), ((), ()))
    both = jnp.concatenate([tokens, out_grad], 1)
    both = gather_a2a(both, ("y", "zl"), nsec // 2, 0)
    both = both.reshape((nsec // 2, 1, -1) + both.shape[1:])
    both = gather_a2a(both, "c", 2, 1).reshape((-1,) + both.shape[3:])
    all_tokens, all_grads = both[:, : tokens.shape[1]], both[:, tokens.shape[1] :]
    total = all_tokens.shape[0]
    edges = [0, total * 2 // 3, total]
    chunks = []
    for c in range(2):
        tok = all_tokens[edges[c] : edges[c + 1]]
        grd = all_grads[edges[c] : edges[c + 1]]
        gate_part = jnp.dot(tok, gate_weight, preferred_element_type=jnp.float32)
        up_part = jnp.dot(tok, up_weight, preferred_element_type=jnp.float32)
        hidden_part = lax.dot_general(
            grd, down_weight, contract_last, preferred_element_type=jnp.float32
        )
        p = jnp.stack([gate_part, up_part, hidden_part])
        p = scatter_sum(p, "x", nx, 1)
        p = scatter_permute(p, "zh", nzh, 1)
        d = jnp.stack(swiglu_grads(p[0], p[1], p[2]))
        d = gather_permute(d, "zh", nzh, 1)
        chunks.append(gather_a2a(d, "x", nx, 1))
    deltas = jnp.concatenate(chunks, 1)
    hidden, gate_delta, up_delta = deltas[0], deltas[1], deltas[2]
    grad_down = lax.dot_general(
        hidden, all_grads, contract_first, preferred_element_type=jnp.float32
    ).astype(jnp.bfloat16)
    grad_gate = lax.dot_general(
        all_tokens, gate_delta, contract_first, preferred_element_type=jnp.float32
    ).astype(jnp.bfloat16)
    grad_up = lax.dot_general(
        all_tokens, up_delta, contract_first, preferred_element_type=jnp.float32
    ).astype(jnp.bfloat16)
    result = lax.dot_general(
        gate_delta, gate_weight, contract_last, preferred_element_type=jnp.float32
    ) + lax.dot_general(up_delta, up_weight, contract_last, preferred_element_type=jnp.float32)
    result = result.reshape((nsec // 2, 2, -1) + result.shape[1:])
    result = scatter_sum(result, "c", 2, 1).reshape((-1,) + result.shape[3:])
    grad_input = scatter_sum(result, ("y", "zl"), nsec // 2, 0).astype(jnp.bfloat16)
    return (grad_input, grad_gate, grad_up, grad_down)


def solution(mesh):
    nsec, nten = mesh.shape["section"], mesh.shape["tensor"]
    nzh = 4
    nx = nten // nzh
    fine = Mesh(mesh.devices.reshape(nsec // 4, 2, 2, nx, nzh), ("y", "zl", "c", "x", "zh"))
    act = P(SEC, TEN)
    wt = P(TEN, SEC)

    def body(*args):
        return local(*args, nx=nx, nzh=nzh, nsec=nsec)

    return jax.shard_map(
        body,
        mesh=fine,
        in_specs=(act, act, wt, wt, act),
        out_specs=(act, wt, wt, act),
        check_vma=False,
    )
```

```python
import jax
import jax.numpy as jnp
from jax import lax
from jax.sharding import Mesh, PartitionSpec as P


def swiglu_grads(gate_value, up_value, hidden_grad):
    logistic = jax.nn.sigmoid(gate_value)
    swish = gate_value * logistic
    hidden = (swish * up_value).astype(jnp.bfloat16)
    up_delta = (hidden_grad * swish).astype(jnp.bfloat16)
    gate_delta = (hidden_grad * up_value * logistic * (1.0 + gate_value * (1.0 - logistic))).astype(
        jnp.bfloat16
    )
    return (hidden, gate_delta, up_delta)


SEC = ("y", "zl", "c")
TEN = ("x", "zh")


def scatter_sum(v, axis_name, n, dim):
    shape = v.shape
    v = v.reshape(shape[:dim] + (n, shape[dim] // n) + shape[dim + 1 :])
    v = lax.all_to_all(v, axis_name, dim, dim, tiled=True)
    return v.sum(dim)


def gather_a2a(v, axis_name, n, dim):
    shape = v.shape
    v = jnp.broadcast_to(jnp.expand_dims(v, dim), shape[:dim] + (n,) + shape[dim:])
    v = lax.all_to_all(v, axis_name, dim, dim, tiled=True)
    return v.reshape(shape[:dim] + (n * shape[dim],) + shape[dim + 1 :])


def scatter_permute(v, axis_name, n, dim):
    me = lax.axis_index(axis_name)
    shape = v.shape
    size = shape[dim] // n
    total = lax.dynamic_slice_in_dim(v, me * size, size, dim)
    for k in range(1, n):
        part = lax.dynamic_slice_in_dim(v, ((me + k) % n) * size, size, dim)
        total = total + lax.ppermute(part, axis_name, [(j, (j + k) % n) for j in range(n)])
    return total


def gather_permute(v, axis_name, n, dim):
    me = lax.axis_index(axis_name)
    got = [v] + [
        lax.ppermute(v, axis_name, [(j, (j + k) % n) for j in range(n)]) for k in range(1, n)
    ]
    ordered = jnp.stack([got[0]] + got[:0:-1])
    ordered = jnp.roll(ordered, me, axis=0)
    ordered = jnp.moveaxis(ordered, 0, dim)
    shape = v.shape
    return ordered.reshape(shape[:dim] + (n * shape[dim],) + shape[dim + 1 :])


def local(tokens, out_grad, gate_weight, up_weight, down_weight, nx, nzh, nsec):
    contract_last = (((1,), (1,)), ((), ()))
    contract_first = (((0,), (0,)), ((), ()))
    both = jnp.concatenate([tokens, out_grad], 1)
    both = gather_a2a(both, ("y", "zl"), nsec // 2, 0)
    both = both.reshape((nsec // 2, 1, -1) + both.shape[1:])
    both = gather_a2a(both, "c", 2, 1).reshape((-1,) + both.shape[3:])
    all_tokens, all_grads = both[:, : tokens.shape[1]], both[:, tokens.shape[1] :]
    rows = all_tokens.shape[0] // 2
    chunks = []
    for c in range(2):
        tok = all_tokens[c * rows : (c + 1) * rows]
        grd = all_grads[c * rows : (c + 1) * rows]
        gate_part = jnp.dot(tok, gate_weight, preferred_element_type=jnp.float32)
        up_part = jnp.dot(tok, up_weight, preferred_element_type=jnp.float32)
        hidden_part = lax.dot_general(
            grd, down_weight, contract_last, preferred_element_type=jnp.float32
        )
        p = jnp.stack([gate_part, up_part, hidden_part])
        p = scatter_sum(p, "x", nx, 1)
        if c == 0:
            p = scatter_permute(p, "zh", nzh, 1)
        else:
            p = scatter_sum(p, "zh", nzh, 1)
        d = jnp.stack(swiglu_grads(p[0], p[1], p[2]))
        d = gather_permute(d, "zh", nzh, 1)
        chunks.append(gather_a2a(d, "x", nx, 1))
    deltas = jnp.concatenate(chunks, 1)
    hidden, gate_delta, up_delta = deltas[0], deltas[1], deltas[2]
    grad_down = lax.dot_general(
        hidden, all_grads, contract_first, preferred_element_type=jnp.float32
    ).astype(jnp.bfloat16)
    grad_gate = lax.dot_general(
        all_tokens, gate_delta, contract_first, preferred_element_type=jnp.float32
    ).astype(jnp.bfloat16)
    grad_up = lax.dot_general(
        all_tokens, up_delta, contract_first, preferred_element_type=jnp.float32
    ).astype(jnp.bfloat16)
    result = lax.dot_general(
        gate_delta, gate_weight, contract_last, preferred_element_type=jnp.float32
    ) + lax.dot_general(up_delta, up_weight, contract_last, preferred_element_type=jnp.float32)
    result = result.reshape((nsec // 2, 2, -1) + result.shape[1:])
    result = scatter_sum(result, "c", 2, 1).reshape((-1,) + result.shape[3:])
    grad_input = scatter_sum(result, ("y", "zl"), nsec // 2, 0).astype(jnp.bfloat16)
    return (grad_input, grad_gate, grad_up, grad_down)


def solution(mesh):
    nsec, nten = mesh.shape["section"], mesh.shape["tensor"]
    nzh = 4
    nx = nten // nzh
    fine = Mesh(mesh.devices.reshape(nsec // 4, 2, 2, nx, nzh), ("y", "zl", "c", "x", "zh"))
    act = P(SEC, TEN)
    wt = P(TEN, SEC)

    def body(*args):
        return local(*args, nx=nx, nzh=nzh, nsec=nsec)

    return jax.shard_map(
        body,
        mesh=fine,
        in_specs=(act, act, wt, wt, act),
        out_specs=(act, wt, wt, act),
        check_vma=False,
    )
```

```python
import jax
import jax.numpy as jnp
from jax import lax
from jax.sharding import Mesh, PartitionSpec as P


def swiglu_grads(gate_value, up_value, hidden_grad):
    logistic = jax.nn.sigmoid(gate_value)
    swish = gate_value * logistic
    hidden = (swish * up_value).astype(jnp.bfloat16)
    up_delta = (hidden_grad * swish).astype(jnp.bfloat16)
    gate_delta = (hidden_grad * up_value * logistic * (1.0 + gate_value * (1.0 - logistic))).astype(
        jnp.bfloat16
    )
    return (hidden, gate_delta, up_delta)


SEC = ("y", "zl", "c")
TEN = ("x", "zh")


def scatter_sum(v, axis_name, n, dim):
    shape = v.shape
    v = v.reshape(shape[:dim] + (n, shape[dim] // n) + shape[dim + 1 :])
    v = lax.all_to_all(v, axis_name, dim, dim, tiled=True)
    return v.sum(dim)


def gather_a2a(v, axis_name, n, dim):
    shape = v.shape
    v = jnp.broadcast_to(jnp.expand_dims(v, dim), shape[:dim] + (n,) + shape[dim:])
    v = lax.all_to_all(v, axis_name, dim, dim, tiled=True)
    return v.reshape(shape[:dim] + (n * shape[dim],) + shape[dim + 1 :])


def scatter_permute(v, axis_name, n, dim):
    me = lax.axis_index(axis_name)
    shape = v.shape
    size = shape[dim] // n
    total = lax.dynamic_slice_in_dim(v, me * size, size, dim)
    for k in range(1, n):
        part = lax.dynamic_slice_in_dim(v, ((me + k) % n) * size, size, dim)
        total = total + lax.ppermute(part, axis_name, [(j, (j + k) % n) for j in range(n)])
    return total


def gather_permute(v, axis_name, n, dim):
    me = lax.axis_index(axis_name)
    got = [v] + [
        lax.ppermute(v, axis_name, [(j, (j + k) % n) for j in range(n)]) for k in range(1, n)
    ]
    ordered = jnp.stack([got[0]] + got[:0:-1])
    ordered = jnp.roll(ordered, me, axis=0)
    ordered = jnp.moveaxis(ordered, 0, dim)
    shape = v.shape
    return ordered.reshape(shape[:dim] + (n * shape[dim],) + shape[dim + 1 :])


def local(tokens, out_grad, gate_weight, up_weight, down_weight, nx, nzh, nsec):
    contract_last = (((1,), (1,)), ((), ()))
    contract_first = (((0,), (0,)), ((), ()))
    both = jnp.concatenate([tokens, out_grad], 1)
    mine = gather_a2a(both, ("y", "zl"), nsec // 2, 0)
    swap = [(0, 1), (1, 0)]
    parts_in = [mine, lax.ppermute(mine, "c", swap)]
    width = tokens.shape[1]
    chunks = []
    for rows in parts_in:
        tok, grd = rows[:, :width], rows[:, width:]
        gate_part = jnp.dot(tok, gate_weight, preferred_element_type=jnp.float32)
        up_part = jnp.dot(tok, up_weight, preferred_element_type=jnp.float32)
        hidden_part = lax.dot_general(
            grd, down_weight, contract_last, preferred_element_type=jnp.float32
        )
        p = jnp.stack([gate_part, up_part, hidden_part])
        p = scatter_sum(p, "x", nx, 1)
        p = scatter_permute(p, "zh", nzh, 1)
        d = jnp.stack(swiglu_grads(p[0], p[1], p[2]))
        d = gather_permute(d, "zh", nzh, 1)
        chunks.append(gather_a2a(d, "x", nx, 1))
    deltas = jnp.concatenate(chunks, 1)
    both = jnp.concatenate(parts_in, 0)
    all_tokens, all_grads = both[:, :width], both[:, width:]
    hidden, gate_delta, up_delta = deltas[0], deltas[1], deltas[2]
    grad_down = lax.dot_general(
        hidden, all_grads, contract_first, preferred_element_type=jnp.float32
    ).astype(jnp.bfloat16)
    grad_gate = lax.dot_general(
        all_tokens, gate_delta, contract_first, preferred_element_type=jnp.float32
    ).astype(jnp.bfloat16)
    grad_up = lax.dot_general(
        all_tokens, up_delta, contract_first, preferred_element_type=jnp.float32
    ).astype(jnp.bfloat16)
    result = lax.dot_general(
        gate_delta, gate_weight, contract_last, preferred_element_type=jnp.float32
    ) + lax.dot_general(up_delta, up_weight, contract_last, preferred_element_type=jnp.float32)
    half = result.shape[0] // 2
    result = result[:half] + lax.ppermute(result[half:], "c", swap)
    grad_input = scatter_sum(result, ("y", "zl"), nsec // 2, 0).astype(jnp.bfloat16)
    return (grad_input, grad_gate, grad_up, grad_down)


def solution(mesh):
    nsec, nten = mesh.shape["section"], mesh.shape["tensor"]
    nzh = 4
    nx = nten // nzh
    fine = Mesh(mesh.devices.reshape(nsec // 4, 2, 2, nx, nzh), ("y", "zl", "c", "x", "zh"))
    act = P(SEC, TEN)
    wt = P(TEN, SEC)

    def body(*args):
        return local(*args, nx=nx, nzh=nzh, nsec=nsec)

    return jax.shard_map(
        body,
        mesh=fine,
        in_specs=(act, act, wt, wt, act),
        out_specs=(act, wt, wt, act),
        check_vma=False,
    )
```

```python
import jax
import jax.numpy as jnp
from jax import lax
from jax.sharding import Mesh, PartitionSpec as P


def swiglu_grads(gate_value, up_value, hidden_grad):
    logistic = jax.nn.sigmoid(gate_value)
    swish = gate_value * logistic
    hidden = (swish * up_value).astype(jnp.bfloat16)
    up_delta = (hidden_grad * swish).astype(jnp.bfloat16)
    gate_delta = (hidden_grad * up_value * logistic * (1.0 + gate_value * (1.0 - logistic))).astype(
        jnp.bfloat16
    )
    return (hidden, gate_delta, up_delta)


SEC = ("y", "zl", "c")
TEN = ("x", "zh")


def scatter_sum(v, axis_name, n, dim):
    shape = v.shape
    v = v.reshape(shape[:dim] + (n, shape[dim] // n) + shape[dim + 1 :])
    v = lax.all_to_all(v, axis_name, dim, dim, tiled=True)
    return v.sum(dim)


def gather_a2a(v, axis_name, n, dim):
    shape = v.shape
    v = jnp.broadcast_to(jnp.expand_dims(v, dim), shape[:dim] + (n,) + shape[dim:])
    v = lax.all_to_all(v, axis_name, dim, dim, tiled=True)
    return v.reshape(shape[:dim] + (n * shape[dim],) + shape[dim + 1 :])


def scatter_permute(v, axis_name, n, dim):
    me = lax.axis_index(axis_name)
    shape = v.shape
    size = shape[dim] // n
    total = lax.dynamic_slice_in_dim(v, me * size, size, dim)
    for k in range(1, n):
        part = lax.dynamic_slice_in_dim(v, ((me + k) % n) * size, size, dim)
        total = total + lax.ppermute(part, axis_name, [(j, (j + k) % n) for j in range(n)])
    return total


def gather_permute(v, axis_name, n, dim):
    me = lax.axis_index(axis_name)
    got = [v] + [
        lax.ppermute(v, axis_name, [(j, (j + k) % n) for j in range(n)]) for k in range(1, n)
    ]
    ordered = jnp.stack([got[0]] + got[:0:-1])
    ordered = jnp.roll(ordered, me, axis=0)
    ordered = jnp.moveaxis(ordered, 0, dim)
    shape = v.shape
    return ordered.reshape(shape[:dim] + (n * shape[dim],) + shape[dim + 1 :])


def local(tokens, out_grad, gate_weight, up_weight, down_weight, nx, nzh, nsec):
    contract_last = (((1,), (1,)), ((), ()))
    contract_first = (((0,), (0,)), ((), ()))
    both = jnp.concatenate([tokens, out_grad], 1)
    mine = gather_a2a(both, ("y", "zl"), nsec // 2, 0)
    swap = [(0, 1), (1, 0)]
    parts_in = [mine, lax.ppermute(mine, "c", swap)]
    width = tokens.shape[1]
    chunks = []
    for rows in parts_in:
        rows = rows.reshape((nx, -1) + rows.shape[1:])
        tok, grd = rows[..., :width], rows[..., width:]
        gate_part = jnp.einsum("brd,dh->brh", tok, gate_weight, preferred_element_type=jnp.float32)
        up_part = jnp.einsum("brd,dh->brh", tok, up_weight, preferred_element_type=jnp.float32)
        hidden_part = jnp.einsum("brd,hd->brh", grd, down_weight, preferred_element_type=jnp.float32)
        p = jnp.stack([gate_part, up_part, hidden_part], 1)
        p = lax.all_to_all(p, "x", 0, 0, tiled=True).sum(0)
        p = scatter_permute(p, "zh", nzh, 1)
        d = jnp.stack(swiglu_grads(p[0], p[1], p[2]))
        d = gather_permute(d, "zh", nzh, 1)
        chunks.append(gather_a2a(d, "x", nx, 1))
    deltas = jnp.concatenate(chunks, 1)
    both = jnp.concatenate(parts_in, 0)
    all_tokens, all_grads = both[:, :width], both[:, width:]
    hidden, gate_delta, up_delta = deltas[0], deltas[1], deltas[2]
    grad_down = lax.dot_general(
        hidden, all_grads, contract_first, preferred_element_type=jnp.float32
    ).astype(jnp.bfloat16)
    grad_gate = lax.dot_general(
        all_tokens, gate_delta, contract_first, preferred_element_type=jnp.float32
    ).astype(jnp.bfloat16)
    grad_up = lax.dot_general(
        all_tokens, up_delta, contract_first, preferred_element_type=jnp.float32
    ).astype(jnp.bfloat16)
    result = lax.dot_general(
        gate_delta, gate_weight, contract_last, preferred_element_type=jnp.float32
    ) + lax.dot_general(up_delta, up_weight, contract_last, preferred_element_type=jnp.float32)
    half = result.shape[0] // 2
    result = result[:half] + lax.ppermute(result[half:], "c", swap)
    grad_input = scatter_sum(result, ("y", "zl"), nsec // 2, 0).astype(jnp.bfloat16)
    return (grad_input, grad_gate, grad_up, grad_down)


def solution(mesh):
    nsec, nten = mesh.shape["section"], mesh.shape["tensor"]
    nzh = 4
    nx = nten // nzh
    fine = Mesh(mesh.devices.reshape(nsec // 4, 2, 2, nx, nzh), ("y", "zl", "c", "x", "zh"))
    act = P(SEC, TEN)
    wt = P(TEN, SEC)

    def body(*args):
        return local(*args, nx=nx, nzh=nzh, nsec=nsec)

    return jax.shard_map(
        body,
        mesh=fine,
        in_specs=(act, act, wt, wt, act),
        out_specs=(act, wt, wt, act),
        check_vma=False,
    )
```

```python
import jax
import jax.numpy as jnp
from jax import lax
from jax.sharding import Mesh, PartitionSpec as P


def swiglu_grads(gate_value, up_value, hidden_grad):
    logistic = jax.nn.sigmoid(gate_value)
    swish = gate_value * logistic
    hidden = (swish * up_value).astype(jnp.bfloat16)
    up_delta = (hidden_grad * swish).astype(jnp.bfloat16)
    gate_delta = (hidden_grad * up_value * logistic * (1.0 + gate_value * (1.0 - logistic))).astype(
        jnp.bfloat16
    )
    return (hidden, gate_delta, up_delta)


SEC = ("y", "zl", "c")
TEN = ("x", "zh")


def scatter_sum(v, axis_name, n, dim):
    shape = v.shape
    v = v.reshape(shape[:dim] + (n, shape[dim] // n) + shape[dim + 1 :])
    v = lax.all_to_all(v, axis_name, dim, dim, tiled=True)
    return v.sum(dim)


def gather_a2a(v, axis_name, n, dim):
    shape = v.shape
    v = jnp.broadcast_to(jnp.expand_dims(v, dim), shape[:dim] + (n,) + shape[dim:])
    v = lax.all_to_all(v, axis_name, dim, dim, tiled=True)
    return v.reshape(shape[:dim] + (n * shape[dim],) + shape[dim + 1 :])


def scatter_permute(v, axis_name, n, dim):
    me = lax.axis_index(axis_name)
    shape = v.shape
    size = shape[dim] // n
    total = lax.dynamic_slice_in_dim(v, me * size, size, dim)
    for k in range(1, n):
        part = lax.dynamic_slice_in_dim(v, ((me + k) % n) * size, size, dim)
        total = total + lax.ppermute(part, axis_name, [(j, (j + k) % n) for j in range(n)])
    return total


def gather_permute(v, axis_name, n, dim):
    me = lax.axis_index(axis_name)
    got = [v] + [
        lax.ppermute(v, axis_name, [(j, (j + k) % n) for j in range(n)]) for k in range(1, n)
    ]
    ordered = jnp.stack([got[0]] + got[:0:-1])
    ordered = jnp.roll(ordered, me, axis=0)
    ordered = jnp.moveaxis(ordered, 0, dim)
    shape = v.shape
    return ordered.reshape(shape[:dim] + (n * shape[dim],) + shape[dim + 1 :])


def local(tokens, out_grad, gate_weight, up_weight, down_weight, nx, nzh, nsec):
    contract_last = (((1,), (1,)), ((), ()))
    contract_first = (((0,), (0,)), ((), ()))
    both = jnp.concatenate([tokens, out_grad], 1)
    mine = gather_a2a(both, ("y", "zl"), nsec // 2, 0)
    swap = [(0, 1), (1, 0)]
    parts_in = [mine, lax.ppermute(mine, "c", swap)]
    width = tokens.shape[1]
    chunks = []
    for rows in parts_in:
        rows = rows.reshape((nx, -1) + rows.shape[1:])
        tok, grd = rows[..., :width], rows[..., width:]
        gate_part = jnp.einsum("brd,dh->brh", tok, gate_weight, preferred_element_type=jnp.float32)
        up_part = jnp.einsum("brd,dh->brh", tok, up_weight, preferred_element_type=jnp.float32)
        hidden_part = jnp.einsum("brd,hd->brh", grd, down_weight, preferred_element_type=jnp.float32)
        p = jnp.stack([gate_part, up_part, hidden_part], 1)
        p = lax.all_to_all(p, "x", 0, 0, tiled=True).sum(0)
        p = scatter_permute(p, "zh", nzh, 1)
        d = jnp.stack(swiglu_grads(p[0], p[1], p[2]))
        d = gather_permute(d, "zh", nzh, 1)
        d = jnp.broadcast_to(d[None], (nx,) + d.shape)
        chunks.append(lax.all_to_all(d, "x", 0, 0, tiled=True))
    deltas = jnp.stack(
        [jnp.concatenate([c[:, k].reshape((-1,) + c.shape[3:]) for c in chunks], 0) for k in range(3)]
    )
    both = jnp.concatenate(parts_in, 0)
    all_tokens, all_grads = both[:, :width], both[:, width:]
    hidden, gate_delta, up_delta = deltas[0], deltas[1], deltas[2]
    grad_down = lax.dot_general(
        hidden, all_grads, contract_first, preferred_element_type=jnp.float32
    ).astype(jnp.bfloat16)
    grad_gate = lax.dot_general(
        all_tokens, gate_delta, contract_first, preferred_element_type=jnp.float32
    ).astype(jnp.bfloat16)
    grad_up = lax.dot_general(
        all_tokens, up_delta, contract_first, preferred_element_type=jnp.float32
    ).astype(jnp.bfloat16)
    result = lax.dot_general(
        gate_delta, gate_weight, contract_last, preferred_element_type=jnp.float32
    ) + lax.dot_general(up_delta, up_weight, contract_last, preferred_element_type=jnp.float32)
    half = result.shape[0] // 2
    result = result[:half] + lax.ppermute(result[half:], "c", swap)
    grad_input = scatter_sum(result, ("y", "zl"), nsec // 2, 0).astype(jnp.bfloat16)
    return (grad_input, grad_gate, grad_up, grad_down)


def solution(mesh):
    nsec, nten = mesh.shape["section"], mesh.shape["tensor"]
    nzh = 4
    nx = nten // nzh
    fine = Mesh(mesh.devices.reshape(nsec // 4, 2, 2, nx, nzh), ("y", "zl", "c", "x", "zh"))
    act = P(SEC, TEN)
    wt = P(TEN, SEC)

    def body(*args):
        return local(*args, nx=nx, nzh=nzh, nsec=nsec)

    return jax.shard_map(
        body,
        mesh=fine,
        in_specs=(act, act, wt, wt, act),
        out_specs=(act, wt, wt, act),
        check_vma=False,
    )
```

```python
import jax
import jax.numpy as jnp
from jax import lax
from jax.sharding import Mesh, PartitionSpec as P


def swiglu_grads(gate_value, up_value, hidden_grad):
    logistic = jax.nn.sigmoid(gate_value)
    swish = gate_value * logistic
    hidden = (swish * up_value).astype(jnp.bfloat16)
    up_delta = (hidden_grad * swish).astype(jnp.bfloat16)
    gate_delta = (hidden_grad * up_value * logistic * (1.0 + gate_value * (1.0 - logistic))).astype(
        jnp.bfloat16
    )
    return (hidden, gate_delta, up_delta)


SEC = ("y", "zl", "c")
TEN = ("x", "zh")


def scatter_sum(v, axis_name, n, dim):
    shape = v.shape
    v = v.reshape(shape[:dim] + (n, shape[dim] // n) + shape[dim + 1 :])
    v = lax.all_to_all(v, axis_name, dim, dim, tiled=True)
    return v.sum(dim)


def gather_a2a(v, axis_name, n, dim):
    shape = v.shape
    v = jnp.broadcast_to(jnp.expand_dims(v, dim), shape[:dim] + (n,) + shape[dim:])
    v = lax.all_to_all(v, axis_name, dim, dim, tiled=True)
    return v.reshape(shape[:dim] + (n * shape[dim],) + shape[dim + 1 :])


def scatter_permute(v, axis_name, n, dim):
    me = lax.axis_index(axis_name)
    shape = v.shape
    size = shape[dim] // n
    total = lax.dynamic_slice_in_dim(v, me * size, size, dim)
    for k in range(1, n):
        part = lax.dynamic_slice_in_dim(v, ((me + k) % n) * size, size, dim)
        total = total + lax.ppermute(part, axis_name, [(j, (j + k) % n) for j in range(n)])
    return total


def gather_permute(v, axis_name, n, dim):
    me = lax.axis_index(axis_name)
    got = [v] + [
        lax.ppermute(v, axis_name, [(j, (j + k) % n) for j in range(n)]) for k in range(1, n)
    ]
    ordered = jnp.stack([got[0]] + got[:0:-1])
    ordered = jnp.roll(ordered, me, axis=0)
    ordered = jnp.moveaxis(ordered, 0, dim)
    shape = v.shape
    return ordered.reshape(shape[:dim] + (n * shape[dim],) + shape[dim + 1 :])


def local(tokens, out_grad, gate_weight, up_weight, down_weight, nx, nzh, nsec):
    contract_last = (((1,), (1,)), ((), ()))
    contract_first = (((0,), (0,)), ((), ()))
    both = jnp.concatenate([tokens, out_grad], 1)
    mine = gather_a2a(both, ("y", "zl"), nsec // 2, 0)
    swap = [(0, 1), (1, 0)]
    parts_in = [mine, lax.ppermute(mine, "c", swap)]
    width = tokens.shape[1]
    chunks = []
    for rows in parts_in:
        rows = rows.reshape((nx, nzh, -1) + rows.shape[1:])
        tok, grd = rows[..., :width], rows[..., width:]
        gate_part = jnp.einsum("bzrd,dh->bzrh", tok, gate_weight, preferred_element_type=jnp.float32)
        up_part = jnp.einsum("bzrd,dh->bzrh", tok, up_weight, preferred_element_type=jnp.float32)
        hidden_part = jnp.einsum("bzrd,hd->bzrh", grd, down_weight, preferred_element_type=jnp.float32)
        p = jnp.stack([gate_part, up_part, hidden_part], 2)
        p = lax.all_to_all(p, "x", 0, 0, tiled=True).sum(0)
        p = scatter_permute(p, "zh", nzh, 0)[0]
        d = jnp.stack(swiglu_grads(p[0], p[1], p[2]))
        d = gather_permute(d, "zh", nzh, 1)
        chunks.append(gather_a2a(d, "x", nx, 1))
    deltas = jnp.concatenate(chunks, 1)
    both = jnp.concatenate(parts_in, 0)
    all_tokens, all_grads = both[:, :width], both[:, width:]
    hidden, gate_delta, up_delta = deltas[0], deltas[1], deltas[2]
    grad_down = lax.dot_general(
        hidden, all_grads, contract_first, preferred_element_type=jnp.float32
    ).astype(jnp.bfloat16)
    grad_gate = lax.dot_general(
        all_tokens, gate_delta, contract_first, preferred_element_type=jnp.float32
    ).astype(jnp.bfloat16)
    grad_up = lax.dot_general(
        all_tokens, up_delta, contract_first, preferred_element_type=jnp.float32
    ).astype(jnp.bfloat16)
    result = lax.dot_general(
        gate_delta, gate_weight, contract_last, preferred_element_type=jnp.float32
    ) + lax.dot_general(up_delta, up_weight, contract_last, preferred_element_type=jnp.float32)
    half = result.shape[0] // 2
    result = result[:half] + lax.ppermute(result[half:], "c", swap)
    grad_input = scatter_sum(result, ("y", "zl"), nsec // 2, 0).astype(jnp.bfloat16)
    return (grad_input, grad_gate, grad_up, grad_down)


def solution(mesh):
    nsec, nten = mesh.shape["section"], mesh.shape["tensor"]
    nzh = 4
    nx = nten // nzh
    fine = Mesh(mesh.devices.reshape(nsec // 4, 2, 2, nx, nzh), ("y", "zl", "c", "x", "zh"))
    act = P(SEC, TEN)
    wt = P(TEN, SEC)

    def body(*args):
        return local(*args, nx=nx, nzh=nzh, nsec=nsec)

    return jax.shard_map(
        body,
        mesh=fine,
        in_specs=(act, act, wt, wt, act),
        out_specs=(act, wt, wt, act),
        check_vma=False,
    )
```

```python
import jax
import jax.numpy as jnp
from jax import lax
from jax.sharding import Mesh, PartitionSpec as P


def swiglu_grads(gate_value, up_value, hidden_grad):
    logistic = jax.nn.sigmoid(gate_value)
    swish = gate_value * logistic
    hidden = (swish * up_value).astype(jnp.bfloat16)
    up_delta = (hidden_grad * swish).astype(jnp.bfloat16)
    gate_delta = (hidden_grad * up_value * logistic * (1.0 + gate_value * (1.0 - logistic))).astype(
        jnp.bfloat16
    )
    return (hidden, gate_delta, up_delta)


SEC = ("y", "zl", "c")
TEN = ("x", "zh")


def scatter_sum(v, axis_name, n, dim):
    shape = v.shape
    v = v.reshape(shape[:dim] + (n, shape[dim] // n) + shape[dim + 1 :])
    v = lax.all_to_all(v, axis_name, dim, dim, tiled=True)
    return v.sum(dim)


def gather_a2a(v, axis_name, n, dim):
    shape = v.shape
    v = jnp.broadcast_to(jnp.expand_dims(v, dim), shape[:dim] + (n,) + shape[dim:])
    v = lax.all_to_all(v, axis_name, dim, dim, tiled=True)
    return v.reshape(shape[:dim] + (n * shape[dim],) + shape[dim + 1 :])


def scatter_permute(v, axis_name, n, dim):
    me = lax.axis_index(axis_name)
    shape = v.shape
    size = shape[dim] // n
    total = lax.dynamic_slice_in_dim(v, me * size, size, dim)
    for k in range(1, n):
        part = lax.dynamic_slice_in_dim(v, ((me + k) % n) * size, size, dim)
        total = total + lax.ppermute(part, axis_name, [(j, (j + k) % n) for j in range(n)])
    return total


def gather_permute(v, axis_name, n, dim):
    me = lax.axis_index(axis_name)
    got = [v] + [
        lax.ppermute(v, axis_name, [(j, (j + k) % n) for j in range(n)]) for k in range(1, n)
    ]
    ordered = jnp.stack([got[0]] + got[:0:-1])
    ordered = jnp.roll(ordered, me, axis=0)
    ordered = jnp.moveaxis(ordered, 0, dim)
    shape = v.shape
    return ordered.reshape(shape[:dim] + (n * shape[dim],) + shape[dim + 1 :])


def local(tokens, out_grad, gate_weight, up_weight, down_weight, nx, nzh, nsec):
    contract_last = (((1,), (1,)), ((), ()))
    contract_first = (((0,), (0,)), ((), ()))
    both = jnp.concatenate([tokens, out_grad], 1)
    mine = gather_a2a(both, ("y", "zl"), nsec // 2, 0)
    swap = [(0, 1), (1, 0)]
    parts_in = [mine, lax.ppermute(mine, "c", swap)]
    width = tokens.shape[1]
    gate_up_weight = jnp.stack([gate_weight, up_weight])
    chunks = []
    for rows in parts_in:
        rows = rows.reshape((nx, -1) + rows.shape[1:])
        tok, grd = rows[..., :width], rows[..., width:]
        gate_up = jnp.einsum("brd,kdh->bkrh", tok, gate_up_weight, preferred_element_type=jnp.float32)
        hidden_part = jnp.einsum("brd,hd->brh", grd, down_weight, preferred_element_type=jnp.float32)
        p = jnp.concatenate([gate_up, hidden_part[:, None]], 1)
        p = lax.all_to_all(p, "x", 0, 0, tiled=True).sum(0)
        p = scatter_permute(p, "zh", nzh, 1)
        d = jnp.stack(swiglu_grads(p[0], p[1], p[2]))
        d = gather_permute(d, "zh", nzh, 1)
        chunks.append(gather_a2a(d, "x", nx, 1))
    deltas = jnp.concatenate(chunks, 1)
    both = jnp.concatenate(parts_in, 0)
    all_tokens, all_grads = both[:, :width], both[:, width:]
    hidden, gate_delta, up_delta = deltas[0], deltas[1], deltas[2]
    grad_down = lax.dot_general(
        hidden, all_grads, contract_first, preferred_element_type=jnp.float32
    ).astype(jnp.bfloat16)
    grad_gate = lax.dot_general(
        all_tokens, gate_delta, contract_first, preferred_element_type=jnp.float32
    ).astype(jnp.bfloat16)
    grad_up = lax.dot_general(
        all_tokens, up_delta, contract_first, preferred_element_type=jnp.float32
    ).astype(jnp.bfloat16)
    result = lax.dot_general(
        gate_delta, gate_weight, contract_last, preferred_element_type=jnp.float32
    ) + lax.dot_general(up_delta, up_weight, contract_last, preferred_element_type=jnp.float32)
    half = result.shape[0] // 2
    result = result[:half] + lax.ppermute(result[half:], "c", swap)
    grad_input = scatter_sum(result, ("y", "zl"), nsec // 2, 0).astype(jnp.bfloat16)
    return (grad_input, grad_gate, grad_up, grad_down)


def solution(mesh):
    nsec, nten = mesh.shape["section"], mesh.shape["tensor"]
    nzh = 4
    nx = nten // nzh
    fine = Mesh(mesh.devices.reshape(nsec // 4, 2, 2, nx, nzh), ("y", "zl", "c", "x", "zh"))
    act = P(SEC, TEN)
    wt = P(TEN, SEC)

    def body(*args):
        return local(*args, nx=nx, nzh=nzh, nsec=nsec)

    return jax.shard_map(
        body,
        mesh=fine,
        in_specs=(act, act, wt, wt, act),
        out_specs=(act, wt, wt, act),
        check_vma=False,
    )
```

```python
import jax
import jax.numpy as jnp
from jax import lax
from jax.sharding import Mesh, PartitionSpec as P


def swiglu_grads(gate_value, up_value, hidden_grad):
    logistic = jax.nn.sigmoid(gate_value)
    swish = gate_value * logistic
    hidden = (swish * up_value).astype(jnp.bfloat16)
    up_delta = (hidden_grad * swish).astype(jnp.bfloat16)
    gate_delta = (hidden_grad * up_value * logistic * (1.0 + gate_value * (1.0 - logistic))).astype(
        jnp.bfloat16
    )
    return (hidden, gate_delta, up_delta)


SEC = ("y", "zl", "c")
TEN = ("x", "zh")


def scatter_sum(v, axis_name, n, dim):
    shape = v.shape
    v = v.reshape(shape[:dim] + (n, shape[dim] // n) + shape[dim + 1 :])
    v = lax.all_to_all(v, axis_name, dim, dim, tiled=True)
    return v.sum(dim)


def gather_a2a(v, axis_name, n, dim):
    shape = v.shape
    v = jnp.broadcast_to(jnp.expand_dims(v, dim), shape[:dim] + (n,) + shape[dim:])
    v = lax.all_to_all(v, axis_name, dim, dim, tiled=True)
    return v.reshape(shape[:dim] + (n * shape[dim],) + shape[dim + 1 :])


def scatter_permute(v, axis_name, n, dim):
    me = lax.axis_index(axis_name)
    shape = v.shape
    size = shape[dim] // n
    total = lax.dynamic_slice_in_dim(v, me * size, size, dim)
    for k in range(1, n):
        part = lax.dynamic_slice_in_dim(v, ((me + k) % n) * size, size, dim)
        total = total + lax.ppermute(part, axis_name, [(j, (j + k) % n) for j in range(n)])
    return total


def gather_permute(v, axis_name, n, dim):
    me = lax.axis_index(axis_name)
    got = [v] + [
        lax.ppermute(v, axis_name, [(j, (j + k) % n) for j in range(n)]) for k in range(1, n)
    ]
    ordered = jnp.stack([got[0]] + got[:0:-1])
    ordered = jnp.roll(ordered, me, axis=0)
    ordered = jnp.moveaxis(ordered, 0, dim)
    shape = v.shape
    return ordered.reshape(shape[:dim] + (n * shape[dim],) + shape[dim + 1 :])


def local(tokens, out_grad, gate_weight, up_weight, down_weight, nx, nzh, nsec):
    contract_last = (((1,), (1,)), ((), ()))
    contract_first = (((0,), (0,)), ((), ()))
    both = jnp.concatenate([tokens, out_grad], 1)
    mine = gather_a2a(both, ("y", "zl"), nsec // 2, 0)
    swap = [(0, 1), (1, 0)]
    parts_in = [mine, lax.ppermute(mine, "c", swap)]
    width = tokens.shape[1]
    gate_up_weight = jnp.stack([gate_weight, up_weight])
    chunks = []
    for rows in parts_in:
        rows = rows.reshape((nx, -1) + rows.shape[1:])
        tok, grd = rows[..., :width], rows[..., width:]
        gate_up = jnp.einsum("brd,kdh->bkrh", tok, gate_up_weight, preferred_element_type=jnp.float32)
        hidden_part = jnp.einsum("brd,hd->brh", grd, down_weight, preferred_element_type=jnp.float32)
        p = jnp.concatenate([gate_up, hidden_part[:, None]], 1)
        p = lax.all_to_all(p, "x", 0, 0, tiled=True).sum(0)
        p = scatter_permute(p, "zh", nzh, 1)
        d = jnp.stack(swiglu_grads(p[0], p[1], p[2]))
        d = gather_permute(d, "zh", nzh, 1)
        chunks.append(gather_a2a(d, "x", nx, 1))
    deltas = jnp.concatenate(chunks, 1)
    both = jnp.concatenate(parts_in, 0)
    all_tokens, all_grads = both[:, :width], both[:, width:]
    hidden, gate_delta, up_delta = deltas[0], deltas[1], deltas[2]
    grad_down = lax.dot_general(
        hidden, all_grads, contract_first, preferred_element_type=jnp.float32
    ).astype(jnp.bfloat16)
    grad_gate_up = jnp.einsum(
        "rd,krh->kdh", all_tokens, deltas[1:], preferred_element_type=jnp.float32
    ).astype(jnp.bfloat16)
    grad_gate, grad_up = grad_gate_up[0], grad_gate_up[1]
    result = lax.dot_general(
        gate_delta, gate_weight, contract_last, preferred_element_type=jnp.float32
    ) + lax.dot_general(up_delta, up_weight, contract_last, preferred_element_type=jnp.float32)
    half = result.shape[0] // 2
    result = result[:half] + lax.ppermute(result[half:], "c", swap)
    grad_input = scatter_sum(result, ("y", "zl"), nsec // 2, 0).astype(jnp.bfloat16)
    return (grad_input, grad_gate, grad_up, grad_down)


def solution(mesh):
    nsec, nten = mesh.shape["section"], mesh.shape["tensor"]
    nzh = 4
    nx = nten // nzh
    fine = Mesh(mesh.devices.reshape(nsec // 4, 2, 2, nx, nzh), ("y", "zl", "c", "x", "zh"))
    act = P(SEC, TEN)
    wt = P(TEN, SEC)

    def body(*args):
        return local(*args, nx=nx, nzh=nzh, nsec=nsec)

    return jax.shard_map(
        body,
        mesh=fine,
        in_specs=(act, act, wt, wt, act),
        out_specs=(act, wt, wt, act),
        check_vma=False,
    )
```
